256 devices in a mesh: dp: 8 (over y, x_hi), shard: 32 (over x_lo, z, core).
Axes of the slice: x: 4 (x_hi: 2, x_lo: 2; x = x_hi * 2 + x_lo), y: 4, z: 8, core: 2. Of those that a mesh axis runs over, the one named last changes fastest.
Arguments:
- grads: float32 [8, 1, 2, 4096, 4096], P('dp', None, None, None, 'shard'), may hold values from -6 to 6
- params: float32 [1, 2, 4096, 4096], P(None, None, ('dp', 'shard')), may hold values from -0.09375 to 0.09375
- moment_one: float32 [1, 2, 4096, 4096], P(None, None, ('dp', 'shard')), may hold values from -0.75 to 0.75
- moment_two: float32 [1, 2, 4096, 4096], P(None, None, ('dp', 'shard')), may hold values from 1e-05 to 0.01
- relation_ids: int32 [1], replicated, may hold values from 0 to 63
- rates: float32 [64], replicated, may hold values from 0.02 to 0.1
- step_count: int32 [1], replicated, may hold values from 1 to 8
Outputs:
- new_params: float32 [1, 2, 4096, 4096], P(None, None, ('dp', 'shard'))
- new_moment_one: float32 [1, 2, 4096, 4096], P(None, None, ('dp', 'shard'))
- new_moment_two: float32 [1, 2, 4096, 4096], P(None, None, ('dp', 'shard'))
- panels: bfloat16 [1, 2, 4096, 4096], P(None, None, None, 'shard')
The draws below stay inside these ranges and needn't reach their ends.
Inputs may be any that keep to these rules, and one draw needn't show every extreme that they name: `relation_ids`: relation ids are edge types. `step_count`: the step count is positive.
All inputs are finite; a program needn't handle non-finite values.
Results may differ from the reference program's by a relative error of at most 0.001.
Values may be sent and summed in bfloat16 or wider, within the bound.
No kernel may reach another device: no remote copies, remote signals or barrier semaphores. Data moves between devices by JAX's collectives and lax.ppermute only.
A program may use at most 128 MiB of HBM per device.

```python
import math
import jax
import jax.numpy as jnp
from jax import lax

D = 4096
NTYPES = 64
RW = 1
N_DP = 8


def block_scale(own_key, extent, shards, low, largest):
    def one(dim, shards_of):
        draws = jax.random.uniform(jax.random.fold_in(jax.random.fold_in(own_key, 6), dim), (shards_of,), jnp.float32, low / len(shards), largest / len(shards))
        return jnp.repeat(jnp.exp(draws), extent[dim] // shards_of).reshape((-1,) + (1,) * (len(extent) - dim - 1))

    level = one(*shards[0])
    for cut in shards[1:]:
        level = level * one(*cut)
    return level


def bell_draw(own_key, shape, width, most, shards=(), kind=jnp.bfloat16):
    result = width * jax.random.normal(own_key, shape, jnp.float32)
    if shards:
        result = result * block_scale(own_key, shape, shards, -0.22, 0.18)
    return jnp.clip(result, -most, most).astype(kind)


def setup_inputs(seed: int = 0) -> dict:
    streams_of = jax.random.split(jax.random.key(seed), 8)
    return {
        "grads": bell_draw(streams_of[0], (N_DP, RW, 2, D, D), 1.0, 6.0, ((0, 8), (4, 32)), jnp.float32),
        "params": bell_draw(streams_of[1], (RW, 2, D, D), D ** -0.5, 0.09375, ((2, 256),), jnp.float32),
        "moment_one": bell_draw(streams_of[2], (RW, 2, D, D), 0.05, 0.75, ((2, 256),), jnp.float32),
        "moment_two": jnp.clip(jnp.exp(math.log(0.01) - 6.9077553 * jax.random.uniform(streams_of[3], (RW, 2, D, D), jnp.float32) ** block_scale(streams_of[3], (RW, 2, D, D), ((2, 256),), -0.2, 0.2)), 9.999999747378752e-06, 0.01),
        "relation_ids": jax.random.randint(streams_of[4], (RW,), 0, NTYPES).astype(jnp.int32),
        "rates": jnp.clip(jnp.exp(jax.random.uniform(streams_of[5], (NTYPES,), jnp.float32, math.log(0.02), math.log(0.1))), 0.02, 0.1),
        "step_count": jax.random.randint(streams_of[6], (1,), 1, 9).astype(jnp.int32),
    }


def reference(grads, params, moment_one, moment_two, relation_ids, rates, step_count):
    gradient = lax.optimization_barrier(jnp.sum(grads, axis=0)) / N_DP
    onehot = (relation_ids[:, None] == jnp.arange(rates.shape[0], dtype=jnp.int32)[None, :]).astype(jnp.float32)
    learn = lax.optimization_barrier(jnp.sum(onehot * rates[None, :], axis=1))[:, None, None, None]
    new_one = 0.9 * moment_one + 0.1 * gradient
    new_two = 0.95 * moment_two + 0.05 * gradient * gradient
    steps = step_count[0].astype(jnp.float32)
    fix_one = 1.0 - jnp.power(jnp.float32(0.9), steps)
    fix_two = 1.0 - jnp.power(jnp.float32(0.95), steps)
    update = new_one / fix_one / (jnp.sqrt(new_two / fix_two) + 1e-08) + 0.1 * params
    new_params = params - learn * update
    return (new_params, new_one, new_two, new_params.astype(jnp.bfloat16))
```

```python
import jax
import jax.numpy as jnp
from jax import lax
from jax.sharding import PartitionSpec as P


def body(grads, params, moment_one, moment_two, relation_ids, rates, step_count):
    groups = lax.axis_size("dp")
    owners = lax.axis_size("shard")
    relations = grads.shape[1]
    rows = grads.shape[3]
    panel_cols = grads.shape[-1]
    width = panel_cols * owners
    owned = params.shape[2]
    block = rows // groups
    summed = lax.psum_scatter(grads[0], "dp", scatter_dimension=2, tiled=True)
    pieces = summed.reshape(relations, 2, owners, owned, panel_cols)
    moved = lax.all_to_all(pieces, "shard", split_axis=2, concat_axis=2, tiled=True)
    gradient = moved.transpose(0, 1, 3, 2, 4).reshape(relations, 2, owned, width) / groups
    onehot = (relation_ids[:, None] == jnp.arange(rates.shape[0], dtype=jnp.int32)[None, :]).astype(
        jnp.float32
    )
    learn = jnp.sum(onehot * rates[None, :], axis=1)[:, None, None, None]
    new_one = 0.9 * moment_one + 0.1 * gradient
    new_two = 0.95 * moment_two + 0.05 * gradient * gradient
    steps = step_count[0].astype(jnp.float32)
    fix_one = 1.0 - jnp.power(jnp.float32(0.9), steps)
    fix_two = 1.0 - jnp.power(jnp.float32(0.95), steps)
    update = new_one / fix_one / (jnp.sqrt(new_two / fix_two) + 1e-08) + 0.1 * params
    new_params = params - learn * update
    fresh = new_params.astype(jnp.bfloat16).reshape(relations, 2, owned, owners, panel_cols)
    fresh = fresh.transpose(0, 1, 3, 2, 4)
    back = lax.all_to_all(fresh, "shard", split_axis=2, concat_axis=2, tiled=True)
    back = back.reshape(relations, 2, block, panel_cols)
    panels = lax.all_gather(back, "dp", axis=2, tiled=True)
    return (new_params, new_one, new_two, panels)


def solution(mesh):
    in_specs = (
        P("dp", None, None, None, "shard"),
        P(None, None, ("dp", "shard"), None),
        P(None, None, ("dp", "shard"), None),
        P(None, None, ("dp", "shard"), None),
        P(),
        P(),
        P(),
    )
    out_specs = (
        P(None, None, ("dp", "shard"), None),
        P(None, None, ("dp", "shard"), None),
        P(None, None, ("dp", "shard"), None),
        P(None, None, None, "shard"),
    )
    return jax.shard_map(body, mesh=mesh, in_specs=in_specs, out_specs=out_specs, check_vma=False)
```

```python
import jax
import jax.numpy as jnp
from jax import lax
from jax.sharding import PartitionSpec as P


def _dp_rings(groups):
    ring = groups // 2
    plus = [(2 * y + h, 2 * ((y + 1) % ring) + h) for y in range(ring) for h in range(2)]
    minus = [(2 * y + h, 2 * ((y - 1) % ring) + h) for y in range(ring) for h in range(2)]
    partner = [(2 * y + h, 2 * y + 1 - h) for y in range(ring) for h in range(2)]
    return ring, plus, minus, partner


def _take(x, index):
    return lax.dynamic_index_in_dim(x, index, axis=1, keepdims=False)


def _reduce_scatter_dp(x, groups):
    ring, plus, minus, partner = _dp_rings(groups)
    d = lax.axis_index("dp")
    y = d // 2
    h = d % 2
    even = x[:, :, 0]
    odd = x[:, :, 1]
    up = _take(even, (y - 1) % ring)
    down = _take(odd, (y + 1) % ring)
    for t in range(ring - 1):
        up = lax.ppermute(up, "dp", plus) + _take(even, (y - t - 2) % ring)
        down = lax.ppermute(down, "dp", minus) + _take(odd, (y + t + 2) % ring)
    keep = lax.select(h == 0, up, down)
    send = lax.select(h == 0, down, up)
    return keep + lax.ppermute(send, "dp", partner)


def _all_gather_dp(mine, groups):
    ring, plus, minus, partner = _dp_rings(groups)
    d = lax.axis_index("dp")
    y = d // 2
    h = d % 2
    other = lax.ppermute(mine, "dp", partner)
    even = lax.select(h == 0, mine, other)
    odd = lax.select(h == 0, other, mine)
    lead, block, cols = mine.shape
    out = jnp.zeros((lead, ring, 2, block, cols), mine.dtype)
    out = lax.dynamic_update_slice(out, jnp.stack([even, odd], axis=1)[:, None], (0, y, 0, 0, 0))
    up, down = even, odd
    for t in range(ring - 1):
        up = lax.ppermute(up, "dp", plus)
        down = lax.ppermute(down, "dp", minus)
        out = lax.dynamic_update_slice(out, up[:, None, None], (0, (y - t - 1) % ring, 0, 0, 0))
        out = lax.dynamic_update_slice(out, down[:, None, None], (0, (y + t + 1) % ring, 1, 0, 0))
    return out.reshape(lead, groups * block, cols)


def body(grads, params, moment_one, moment_two, relation_ids, rates, step_count):
    groups = lax.axis_size("dp")
    owners = lax.axis_size("shard")
    relations = grads.shape[1]
    rows = grads.shape[3]
    panel_cols = grads.shape[-1]
    width = panel_cols * owners
    owned = params.shape[2]
    block = rows // groups
    lead = relations * 2
    local = grads.reshape(lead, groups // 2, 2, block, panel_cols)
    summed = _reduce_scatter_dp(local, groups)
    pieces = summed.reshape(relations, 2, owners, owned, panel_cols)
    moved = lax.all_to_all(pieces, "shard", split_axis=2, concat_axis=2, tiled=True)
    gradient = moved.transpose(0, 1, 3, 2, 4).reshape(relations, 2, owned, width) / groups
    onehot = (relation_ids[:, None] == jnp.arange(rates.shape[0], dtype=jnp.int32)[None, :]).astype(
        jnp.float32
    )
    learn = jnp.sum(onehot * rates[None, :], axis=1)[:, None, None, None]
    new_one = 0.9 * moment_one + 0.1 * gradient
    new_two = 0.95 * moment_two + 0.05 * gradient * gradient
    steps = step_count[0].astype(jnp.float32)
    fix_one = 1.0 - jnp.power(jnp.float32(0.9), steps)
    fix_two = 1.0 - jnp.power(jnp.float32(0.95), steps)
    update = new_one / fix_one / (jnp.sqrt(new_two / fix_two) + 1e-08) + 0.1 * params
    new_params = params - learn * update
    fresh = new_params.astype(jnp.bfloat16).reshape(relations, 2, owned, owners, panel_cols)
    fresh = fresh.transpose(0, 1, 3, 2, 4)
    back = lax.all_to_all(fresh, "shard", split_axis=2, concat_axis=2, tiled=True)
    back = back.reshape(lead, block, panel_cols)
    panels = _all_gather_dp(back, groups).reshape(relations, 2, rows, panel_cols)
    return (new_params, new_one, new_two, panels)


def solution(mesh):
    in_specs = (
        P("dp", None, None, None, "shard"),
        P(None, None, ("dp", "shard"), None),
        P(None, None, ("dp", "shard"), None),
        P(None, None, ("dp", "shard"), None),
        P(),
        P(),
        P(),
    )
    out_specs = (
        P(None, None, ("dp", "shard"), None),
        P(None, None, ("dp", "shard"), None),
        P(None, None, ("dp", "shard"), None),
        P(None, None, None, "shard"),
    )
    return jax.shard_map(body, mesh=mesh, in_specs=in_specs, out_specs=out_specs, check_vma=False)
```

```python
import jax
import jax.numpy as jnp
from jax import lax
from jax.sharding import PartitionSpec as P


def _dp_rings(groups):
    ring = groups // 2
    plus = [(2 * y + h, 2 * ((y + 1) % ring) + h) for y in range(ring) for h in range(2)]
    minus = [(2 * y + h, 2 * ((y - 1) % ring) + h) for y in range(ring) for h in range(2)]
    partner = [(2 * y + h, 2 * y + 1 - h) for y in range(ring) for h in range(2)]
    return ring, plus, minus, partner


def _take(x, index):
    return lax.dynamic_index_in_dim(x, index, axis=1, keepdims=False)


def _ring_sum(chunks, y, ring, perm, sign):
    acc = _take(chunks, (y - sign) % ring)
    for t in range(ring - 1):
        acc = lax.ppermute(acc, "dp", perm) + _take(chunks, (y - sign * (t + 2)) % ring)
    return acc


def _reduce_scatter_dp(x, groups):
    ring, plus, minus, partner = _dp_rings(groups)
    d = lax.axis_index("dp")
    y = d // 2
    h = d % 2
    half = x.shape[0] // 2
    rows = x.shape[3] // 2
    first = x[:half]
    up = _ring_sum(first[:, :, 0], y, ring, plus, 1)
    down = _ring_sum(first[:, :, 1], y, ring, minus, -1)
    keep = lax.select(h == 0, up, down)
    send = lax.select(h == 0, down, up)
    done_first = keep + lax.ppermute(send, "dp", partner)
    second = x[half:]
    mine = lax.select(h == 0, second[:, :, 0], second[:, :, 1])
    theirs = lax.select(h == 0, second[:, :, 1], second[:, :, 0])
    paired = mine + lax.ppermute(theirs, "dp", partner)
    top = _ring_sum(paired[:, :, :rows], y, ring, plus, 1)
    bottom = _ring_sum(paired[:, :, rows:], y, ring, minus, -1)
    done_second = jnp.concatenate([top, bottom], axis=1)
    return jnp.concatenate([done_first, done_second], axis=0)


def _all_gather_dp(mine, groups):
    ring, plus, minus, partner = _dp_rings(groups)
    d = lax.axis_index("dp")
    y = d // 2
    h = d % 2
    lead, block, cols = mine.shape
    half = lead // 2
    rows = block // 2
    first = mine[:half]
    other = lax.ppermute(first, "dp", partner)
    even = lax.select(h == 0, first, other)
    odd = lax.select(h == 0, other, first)
    out = jnp.zeros((half, ring, 2, block, cols), mine.dtype)
    out = lax.dynamic_update_slice(out, jnp.stack([even, odd], axis=1)[:, None], (0, y, 0, 0, 0))
    up, down = even, odd
    for t in range(ring - 1):
        up = lax.ppermute(up, "dp", plus)
        down = lax.ppermute(down, "dp", minus)
        out = lax.dynamic_update_slice(out, up[:, None, None], (0, (y - t - 1) % ring, 0, 0, 0))
        out = lax.dynamic_update_slice(out, down[:, None, None], (0, (y + t + 1) % ring, 1, 0, 0))
    panel_first = out.reshape(half, groups * block, cols)
    second = mine[half:]
    ours = jnp.zeros((lead - half, ring, block, cols), mine.dtype)
    ours = lax.dynamic_update_slice(ours, second[:, None], (0, y, 0, 0))
    top = second[:, :rows]
    bottom = second[:, rows:]
    for t in range(ring - 1):
        top = lax.ppermute(top, "dp", plus)
        bottom = lax.ppermute(bottom, "dp", minus)
        ours = lax.dynamic_update_slice(ours, top[:, None], (0, (y - t - 1) % ring, 0, 0))
        ours = lax.dynamic_update_slice(ours, bottom[:, None], (0, (y + t + 1) % ring, rows, 0))
    others = lax.ppermute(ours, "dp", partner)
    even = lax.select(h == 0, ours, others)
    odd = lax.select(h == 0, others, ours)
    panel_second = jnp.stack([even, odd], axis=2).reshape(lead - half, groups * block, cols)
    return jnp.concatenate([panel_first, panel_second], axis=0)


def body(grads, params, moment_one, moment_two, relation_ids, rates, step_count):
    groups = lax.axis_size("dp")
    owners = lax.axis_size("shard")
    relations = grads.shape[1]
    rows = grads.shape[3]
    panel_cols = grads.shape[-1]
    width = panel_cols * owners
    owned = params.shape[2]
    block = rows // groups
    lead = relations * 2
    local = grads.reshape(lead, groups // 2, 2, block, panel_cols)
    summed = _reduce_scatter_dp(local, groups)
    pieces = summed.reshape(relations, 2, owners, owned, panel_cols)
    moved = lax.all_to_all(pieces, "shard", split_axis=2, concat_axis=2, tiled=True)
    gradient = moved.transpose(0, 1, 3, 2, 4).reshape(relations, 2, owned, width) / groups
    onehot = (relation_ids[:, None] == jnp.arange(rates.shape[0], dtype=jnp.int32)[None, :]).astype(
        jnp.float32
    )
    learn = jnp.sum(onehot * rates[None, :], axis=1)[:, None, None, None]
    new_one = 0.9 * moment_one + 0.1 * gradient
    new_two = 0.95 * moment_two + 0.05 * gradient * gradient
    steps = step_count[0].astype(jnp.float32)
    fix_one = 1.0 - jnp.power(jnp.float32(0.9), steps)
    fix_two = 1.0 - jnp.power(jnp.float32(0.95), steps)
    update = new_one / fix_one / (jnp.sqrt(new_two / fix_two) + 1e-08) + 0.1 * params
    new_params = params - learn * update
    fresh = new_params.astype(jnp.bfloat16).reshape(relations, 2, owned, owners, panel_cols)
    fresh = fresh.transpose(0, 1, 3, 2, 4)
    back = lax.all_to_all(fresh, "shard", split_axis=2, concat_axis=2, tiled=True)
    back = back.reshape(lead, block, panel_cols)
    panels = _all_gather_dp(back, groups).reshape(relations, 2, rows, panel_cols)
    return (new_params, new_one, new_two, panels)


def solution(mesh):
    in_specs = (
        P("dp", None, None, None, "shard"),
        P(None, None, ("dp", "shard"), None),
        P(None, None, ("dp", "shard"), None),
        P(None, None, ("dp", "shard"), None),
        P(),
        P(),
        P(),
    )
    out_specs = (
        P(None, None, ("dp", "shard"), None),
        P(None, None, ("dp", "shard"), None),
        P(None, None, ("dp", "shard"), None),
        P(None, None, None, "shard"),
    )
    return jax.shard_map(body, mesh=mesh, in_specs=in_specs, out_specs=out_specs, check_vma=False)
```

```python
import jax
import jax.numpy as jnp
from jax import lax
from jax.sharding import PartitionSpec as P


def _dp_rings(groups):
    ring = groups // 2
    plus = [(2 * y + h, 2 * ((y + 1) % ring) + h) for y in range(ring) for h in range(2)]
    minus = [(2 * y + h, 2 * ((y - 1) % ring) + h) for y in range(ring) for h in range(2)]
    partner = [(2 * y + h, 2 * y + 1 - h) for y in range(ring) for h in range(2)]
    return ring, plus, minus, partner


def _take(x, index):
    return lax.dynamic_index_in_dim(x, index, axis=1, keepdims=False)


def _reduce_scatter_dp(x, groups):
    ring, plus, minus, partner = _dp_rings(groups)
    d = lax.axis_index("dp")
    y = d // 2
    h = d % 2
    even = x[:, :, 0]
    odd = x[:, :, 1]
    up = _take(even, (y - 1) % ring)
    down = _take(odd, (y + 1) % ring)
    for t in range(ring - 1):
        up = lax.ppermute(up, "dp", plus) + _take(even, (y - t - 2) % ring)
        down = lax.ppermute(down, "dp", minus) + _take(odd, (y + t + 2) % ring)
    keep = lax.select(h == 0, up, down)
    send = lax.select(h == 0, down, up)
    return keep + lax.ppermute(send, "dp", partner)


def _all_gather_dp(mine, groups):
    ring, plus, minus, partner = _dp_rings(groups)
    d = lax.axis_index("dp")
    y = d // 2
    h = d % 2
    other = lax.ppermute(mine, "dp", partner)
    even = lax.select(h == 0, mine, other)
    odd = lax.select(h == 0, other, mine)
    lead, block, cols = mine.shape
    out = jnp.zeros((lead, ring, 2, block, cols), mine.dtype)
    out = lax.dynamic_update_slice(out, jnp.stack([even, odd], axis=1)[:, None], (0, y, 0, 0, 0))
    up, down = even, odd
    for t in range(ring - 1):
        up = lax.ppermute(up, "dp", plus)
        down = lax.ppermute(down, "dp", minus)
        out = lax.dynamic_update_slice(out, up[:, None, None], (0, (y - t - 1) % ring, 0, 0, 0))
        out = lax.dynamic_update_slice(out, down[:, None, None], (0, (y + t + 1) % ring, 1, 0, 0))
    return out.reshape(lead, groups * block, cols)


def body(grads, params, moment_one, moment_two, relation_ids, rates, step_count):
    groups = lax.axis_size("dp")
    owners = lax.axis_size("shard")
    relations = grads.shape[1]
    rows = grads.shape[3]
    panel_cols = grads.shape[-1]
    owned = params.shape[2]
    block = rows // groups
    lead = relations * 2
    state = jnp.stack([params, moment_one, moment_two]).reshape(3, relations, 2, owned, owners, panel_cols)
    state = lax.all_to_all(state.transpose(0, 1, 2, 4, 3, 5), "shard", split_axis=3, concat_axis=3, tiled=True)
    state = state.reshape(3, relations, 2, block, panel_cols)
    params_p, one_p, two_p = state[0], state[1], state[2]
    local = grads.reshape(lead, groups // 2, 2, block, panel_cols)
    gradient = _reduce_scatter_dp(local, groups).reshape(relations, 2, block, panel_cols) / groups
    onehot = (relation_ids[:, None] == jnp.arange(rates.shape[0], dtype=jnp.int32)[None, :]).astype(
        jnp.float32
    )
    learn = jnp.sum(onehot * rates[None, :], axis=1)[:, None, None, None]
    new_one = 0.9 * one_p + 0.1 * gradient
    new_two = 0.95 * two_p + 0.05 * gradient * gradient
    steps = step_count[0].astype(jnp.float32)
    fix_one = 1.0 - jnp.power(jnp.float32(0.9), steps)
    fix_two = 1.0 - jnp.power(jnp.float32(0.95), steps)
    update = new_one / fix_one / (jnp.sqrt(new_two / fix_two) + 1e-08) + 0.1 * params_p
    new_params = params_p - learn * update
    fresh = new_params.astype(jnp.bfloat16).reshape(lead, block, panel_cols)
    panels = _all_gather_dp(fresh, groups).reshape(relations, 2, rows, panel_cols)
    out = jnp.stack([new_params, new_one, new_two]).reshape(3, relations, 2, owners, owned, panel_cols)
    out = lax.all_to_all(out, "shard", split_axis=3, concat_axis=3, tiled=True)
    out = out.transpose(0, 1, 2, 4, 3, 5).reshape(3, relations, 2, owned, owners * panel_cols)
    return (out[0], out[1], out[2], panels)


def solution(mesh):
    in_specs = (
        P("dp", None, None, None, "shard"),
        P(None, None, ("dp", "shard"), None),
        P(None, None, ("dp", "shard"), None),
        P(None, None, ("dp", "shard"), None),
        P(),
        P(),
        P(),
    )
    out_specs = (
        P(None, None, ("dp", "shard"), None),
        P(None, None, ("dp", "shard"), None),
        P(None, None, ("dp", "shard"), None),
        P(None, None, None, "shard"),
    )
    return jax.shard_map(body, mesh=mesh, in_specs=in_specs, out_specs=out_specs, check_vma=False)
```

```python
import jax
import jax.numpy as jnp
from jax import lax
from jax.sharding import PartitionSpec as P


def _dp_rings(groups):
    ring = groups // 2
    plus = [(2 * y + h, 2 * ((y + 1) % ring) + h) for y in range(ring) for h in range(2)]
    minus = [(2 * y + h, 2 * ((y - 1) % ring) + h) for y in range(ring) for h in range(2)]
    partner = [(2 * y + h, 2 * y + 1 - h) for y in range(ring) for h in range(2)]
    return ring, plus, minus, partner


def _take(x, index):
    return lax.dynamic_index_in_dim(x, index, axis=1, keepdims=False)


def _reduce_scatter_dp(x, groups):
    ring, plus, minus, partner = _dp_rings(groups)
    d = lax.axis_index("dp")
    y = d // 2
    h = d % 2
    up = _take(x, 2 * ((y - 1) % ring))
    down = _take(x, 2 * ((y + 1) % ring) + 1)
    for t in range(ring - 1):
        up = lax.ppermute(up, "dp", plus)
        down = lax.ppermute(down, "dp", minus)
        up = up + _take(x, 2 * ((y - t - 2) % ring))
        down = down + _take(x, 2 * ((y + t + 2) % ring) + 1)
    keep = lax.select(h == 0, up, down)
    send = lax.select(h == 0, down, up)
    return keep + lax.ppermute(send, "dp", partner)


def _all_gather_dp(mine, groups):
    ring, plus, minus, partner = _dp_rings(groups)
    d = lax.axis_index("dp")
    y = d // 2
    h = d % 2
    lead, block, cols = mine.shape
    rows = block // 2
    ours = jnp.zeros((lead, ring, block, cols), mine.dtype)
    ours = lax.dynamic_update_slice(ours, mine[:, None], (0, y, 0, 0))
    top = mine[:, :rows]
    bottom = mine[:, rows:]
    for t in range(ring - 1):
        top = lax.ppermute(top, "dp", plus)
        bottom = lax.ppermute(bottom, "dp", minus)
        ours = lax.dynamic_update_slice(ours, top[:, None], (0, (y - t - 1) % ring, 0, 0))
        ours = lax.dynamic_update_slice(ours, bottom[:, None], (0, (y + t + 1) % ring, rows, 0))
    others = lax.ppermute(ours, "dp", partner)
    even = lax.select(h == 0, ours, others)
    odd = lax.select(h == 0, others, ours)
    return jnp.stack([even, odd], axis=2).reshape(lead, groups * block, cols)


def _step(grads, params, moment_one, moment_two, relation_ids, rates, step_count):
    groups = lax.axis_size("dp")
    owners = lax.axis_size("shard")
    relations = grads.shape[1]
    rows = grads.shape[3]
    panel_cols = grads.shape[-1]
    owned = params.shape[2]
    block = rows // groups
    lead = relations * 2
    state = jnp.stack([params, moment_one, moment_two]).reshape(3, relations, 2, 1, owned, owners, panel_cols)
    state = lax.all_to_all(state, "shard", split_axis=5, concat_axis=3, tiled=True)
    state = state.reshape(3, relations, 2, block, panel_cols)
    params_p, one_p, two_p = state[0], state[1], state[2]
    local = grads.reshape(lead, groups, block, panel_cols)
    gradient = _reduce_scatter_dp(local, groups).reshape(relations, 2, block, panel_cols) / groups
    onehot = (relation_ids[:, None] == jnp.arange(rates.shape[0], dtype=jnp.int32)[None, :]).astype(
        jnp.float32
    )
    learn = jnp.sum(onehot * rates[None, :], axis=1)[:, None, None, None]
    new_one = 0.9 * one_p + 0.1 * gradient
    new_two = 0.95 * two_p + 0.05 * gradient * gradient
    steps = step_count[0].astype(jnp.float32)
    fix_one = 1.0 - jnp.power(jnp.float32(0.9), steps)
    fix_two = 1.0 - jnp.power(jnp.float32(0.95), steps)
    update = new_one / fix_one / (jnp.sqrt(new_two / fix_two) + 1e-08) + 0.1 * params_p
    new_params = params_p - learn * update
    fresh = new_params.astype(jnp.bfloat16).reshape(lead, block, panel_cols)
    panels = _all_gather_dp(fresh, groups).reshape(relations, 2, rows, panel_cols)
    out = jnp.stack([new_params, new_one, new_two]).reshape(3, relations, 2, owners, owned, 1, panel_cols)
    out = lax.all_to_all(out, "shard", split_axis=3, concat_axis=5, tiled=True)
    out = out.reshape(3, relations, 2, owned, owners * panel_cols)
    return (out[0], out[1], out[2], panels)


def solution(mesh):
    in_specs = (
        P("dp", None, None, None, "shard"),
        P(None, None, ("dp", "shard"), None),
        P(None, None, ("dp", "shard"), None),
        P(None, None, ("dp", "shard"), None),
        P(),
        P(),
        P(),
    )
    out_specs = (
        P(None, None, ("dp", "shard"), None),
        P(None, None, ("dp", "shard"), None),
        P(None, None, ("dp", "shard"), None),
        P(None, None, None, "shard"),
    )
    return jax.shard_map(_step, mesh=mesh, in_specs=in_specs, out_specs=out_specs, check_vma=False)
```

```python
import jax
import jax.numpy as jnp
from jax import lax
from jax.sharding import PartitionSpec as P


def _dp_rings(groups):
    ring = groups // 2
    plus = [(2 * y + h, 2 * ((y + 1) % ring) + h) for y in range(ring) for h in range(2)]
    minus = [(2 * y + h, 2 * ((y - 1) % ring) + h) for y in range(ring) for h in range(2)]
    partner = [(2 * y + h, 2 * y + 1 - h) for y in range(ring) for h in range(2)]
    return ring, plus, minus, partner


def _take(x, index):
    return lax.dynamic_index_in_dim(x, index, axis=1, keepdims=False)


def _reduce_scatter_dp(x, groups):
    ring, plus, minus, partner = _dp_rings(groups)
    d = lax.axis_index("dp")
    y = d // 2
    h = d % 2
    up = _take(x, 2 * ((y - 1) % ring))
    down = _take(x, 2 * ((y + 1) % ring) + 1)
    for t in range(ring - 1):
        up = lax.ppermute(up, "dp", plus)
        down = lax.ppermute(down, "dp", minus)
        up = up + _take(x, 2 * ((y - t - 2) % ring))
        down = down + _take(x, 2 * ((y + t + 2) % ring) + 1)
    keep = lax.select(h == 0, up, down)
    send = lax.select(h == 0, down, up)
    return keep + lax.ppermute(send, "dp", partner)


def _all_gather_dp(mine, groups):
    ring, plus, minus, partner = _dp_rings(groups)
    d = lax.axis_index("dp")
    y = d // 2
    h = d % 2
    other = lax.ppermute(mine, "dp", partner)
    even = lax.select(h == 0, mine, other)
    odd = lax.select(h == 0, other, mine)
    lead, block, cols = mine.shape
    out = jnp.zeros((lead, ring, 2, block, cols), mine.dtype)
    out = lax.dynamic_update_slice(out, jnp.stack([even, odd], axis=1)[:, None], (0, y, 0, 0, 0))
    up, down = even, odd
    for t in range(ring - 1):
        up = lax.ppermute(up, "dp", plus)
        down = lax.ppermute(down, "dp", minus)
        out = lax.dynamic_update_slice(out, up[:, None, None], (0, (y - t - 1) % ring, 0, 0, 0))
        out = lax.dynamic_update_slice(out, down[:, None, None], (0, (y + t + 1) % ring, 1, 0, 0))
    return out.reshape(lead, groups * block, cols)


def _step(grads, params, moment_one, moment_two, relation_ids, rates, step_count):
    groups = lax.axis_size("dp")
    owners = lax.axis_size("shard")
    relations = grads.shape[1]
    rows = grads.shape[3]
    panel_cols = grads.shape[-1]
    owned = params.shape[2]
    block = rows // groups
    lead = relations * 2
    state = jnp.stack([params, moment_one, moment_two]).reshape(3, relations, 2, 1, owned, owners, panel_cols)
    state = lax.all_to_all(state, "shard", split_axis=5, concat_axis=3, tiled=True)
    state = state.reshape(3, relations, 2, block, panel_cols)
    params_p, one_p, two_p = state[0], state[1], state[2]
    local = grads.reshape(lead, groups, block, panel_cols)
    gradient = _reduce_scatter_dp(local, groups).reshape(relations, 2, block, panel_cols) / groups
    onehot = (relation_ids[:, None] == jnp.arange(rates.shape[0], dtype=jnp.int32)[None, :]).astype(
        jnp.float32
    )
    learn = jnp.sum(onehot * rates[None, :], axis=1)[:, None, None, None]
    new_one = 0.9 * one_p + 0.1 * gradient
    new_two = 0.95 * two_p + 0.05 * gradient * gradient
    steps = step_count[0].astype(jnp.float32)
    fix_one = 1.0 - jnp.power(jnp.float32(0.9), steps)
    fix_two = 1.0 - jnp.power(jnp.float32(0.95), steps)
    update = new_one / fix_one / (jnp.sqrt(new_two / fix_two) + 1e-08) + 0.1 * params_p
    new_params = params_p - learn * update
    fresh = new_params.astype(jnp.bfloat16).reshape(lead, block, panel_cols)
    panels = _all_gather_dp(fresh, groups).reshape(relations, 2, rows, panel_cols)
    out = jnp.stack([new_params, new_one, new_two]).reshape(3, relations, 2, owners, owned, 1, panel_cols)
    out = lax.all_to_all(out, "shard", split_axis=3, concat_axis=5, tiled=True)
    out = out.reshape(3, relations, 2, owned, owners * panel_cols)
    return (out[0], out[1], out[2], panels)


def solution(mesh):
    in_specs = (
        P("dp", None, None, None, "shard"),
        P(None, None, ("dp", "shard"), None),
        P(None, None, ("dp", "shard"), None),
        P(None, None, ("dp", "shard"), None),
        P(),
        P(),
        P(),
    )
    out_specs = (
        P(None, None, ("dp", "shard"), None),
        P(None, None, ("dp", "shard"), None),
        P(None, None, ("dp", "shard"), None),
        P(None, None, None, "shard"),
    )
    return jax.shard_map(_step, mesh=mesh, in_specs=in_specs, out_specs=out_specs, check_vma=False)
```

```python
import jax
import jax.numpy as jnp
from jax import lax
from jax.sharding import PartitionSpec as P


def _dp_rings(groups):
    ring = groups // 2
    plus = [(2 * y + h, 2 * ((y + 1) % ring) + h) for y in range(ring) for h in range(2)]
    minus = [(2 * y + h, 2 * ((y - 1) % ring) + h) for y in range(ring) for h in range(2)]
    partner = [(2 * y + h, 2 * y + 1 - h) for y in range(ring) for h in range(2)]
    return ring, plus, minus, partner


def _take(x, index):
    return lax.dynamic_index_in_dim(x, index, axis=1, keepdims=False)


def _reduce_scatter_dp(x, groups):
    ring, plus, minus, partner = _dp_rings(groups)
    d = lax.axis_index("dp")
    y = d // 2
    h = d % 2
    up = _take(x, 2 * ((y - 1) % ring))
    down = _take(x, 2 * ((y + 1) % ring) + 1)
    for t in range(ring - 1):
        up = lax.ppermute(up, "dp", plus)
        down = lax.ppermute(down, "dp", minus)
        up = up + _take(x, 2 * ((y - t - 2) % ring))
        down = down + _take(x, 2 * ((y + t + 2) % ring) + 1)
    keep = lax.select(h == 0, up, down)
    send = lax.select(h == 0, down, up)
    return keep + lax.ppermute(send, "dp", partner)


def _all_gather_dp(mine, groups):
    ring, plus, minus, partner = _dp_rings(groups)
    d = lax.axis_index("dp")
    y = d // 2
    h = d % 2
    other = lax.ppermute(mine, "dp", partner)
    even = lax.select(h == 0, mine, other)
    odd = lax.select(h == 0, other, mine)
    lead, block, cols = mine.shape
    out = jnp.zeros((lead, ring, 2, block, cols), mine.dtype)
    out = lax.dynamic_update_slice(out, jnp.stack([even, odd], axis=1)[:, None], (0, y, 0, 0, 0))
    up, down = even, odd
    for t in range(ring - 1):
        up = lax.ppermute(up, "dp", plus)
        down = lax.ppermute(down, "dp", minus)
        out = lax.dynamic_update_slice(out, up[:, None, None], (0, (y - t - 1) % ring, 0, 0, 0))
        out = lax.dynamic_update_slice(out, down[:, None, None], (0, (y + t + 1) % ring, 1, 0, 0))
    return out.reshape(lead, groups * block, cols)


def _adam(gradient, params, moment_one, moment_two, learn, fix_one, fix_two):
    new_one = 0.9 * moment_one + 0.1 * gradient
    new_two = 0.95 * moment_two + 0.05 * gradient * gradient
    update = new_one / fix_one / (jnp.sqrt(new_two / fix_two) + 1e-08) + 0.1 * params
    return params - learn * update, new_one, new_two


def _step(grads, params, moment_one, moment_two, relation_ids, rates, step_count):
    groups = lax.axis_size("dp")
    owners = lax.axis_size("shard")
    relations = grads.shape[1]
    rows = grads.shape[3]
    panel_cols = grads.shape[-1]
    owned = params.shape[2]
    block = rows // groups
    lead = relations * 2
    onehot = (relation_ids[:, None] == jnp.arange(rates.shape[0], dtype=jnp.int32)[None, :]).astype(
        jnp.float32
    )
    learn = jnp.sum(onehot * rates[None, :], axis=1)[:, None, None, None]
    steps = step_count[0].astype(jnp.float32)
    fix_one = 1.0 - jnp.power(jnp.float32(0.9), steps)
    fix_two = 1.0 - jnp.power(jnp.float32(0.95), steps)
    state = jnp.stack([params, moment_one, moment_two]).reshape(3, relations, 2, 1, owned, owners, panel_cols)
    state = lax.all_to_all(state, "shard", split_axis=5, concat_axis=3, tiled=True)
    state = state.reshape(3, relations, 2, block, panel_cols)
    local = grads.reshape(lead, groups, block, panel_cols)
    ringed = block * 5 // 8
    offload = lax.psum_scatter(local[:, :, ringed:].reshape(lead, -1, panel_cols), "dp", scatter_dimension=1, tiled=True)
    summed = _reduce_scatter_dp(local[:, :, :ringed], groups)
    summed = jnp.concatenate([summed, offload], axis=1)
    gradient = summed.reshape(relations, 2, block, panel_cols) / groups
    fresh, _, _ = _adam(gradient, state[0], state[1], state[2], learn, fix_one, fix_two)
    fresh = fresh.astype(jnp.bfloat16).reshape(lead, block, panel_cols)
    panels = _all_gather_dp(fresh, groups).reshape(relations, 2, rows, panel_cols)
    moved = (summed / groups).reshape(relations, 2, owners, owned, 1, panel_cols)
    moved = lax.all_to_all(moved, "shard", split_axis=2, concat_axis=4, tiled=True)
    moved = moved.reshape(relations, 2, owned, owners * panel_cols)
    new_params, new_one, new_two = _adam(moved, params, moment_one, moment_two, learn, fix_one, fix_two)
    return (new_params, new_one, new_two, panels)


def solution(mesh):
    in_specs = (
        P("dp", None, None, None, "shard"),
        P(None, None, ("dp", "shard"), None),
        P(None, None, ("dp", "shard"), None),
        P(None, None, ("dp", "shard"), None),
        P(),
        P(),
        P(),
    )
    out_specs = (
        P(None, None, ("dp", "shard"), None),
        P(None, None, ("dp", "shard"), None),
        P(None, None, ("dp", "shard"), None),
        P(None, None, None, "shard"),
    )
    return jax.shard_map(_step, mesh=mesh, in_specs=in_specs, out_specs=out_specs, check_vma=False)
```

```python
import jax
import jax.numpy as jnp
from jax import lax
from jax.sharding import PartitionSpec as P


def _dp_rings(groups):
    ring = groups // 2
    plus = [(2 * y + h, 2 * ((y + 1) % ring) + h) for y in range(ring) for h in range(2)]
    minus = [(2 * y + h, 2 * ((y - 1) % ring) + h) for y in range(ring) for h in range(2)]
    partner = [(2 * y + h, 2 * y + 1 - h) for y in range(ring) for h in range(2)]
    return ring, plus, minus, partner


def _take(x, index):
    return lax.dynamic_index_in_dim(x, index, axis=1, keepdims=False)


def _reduce_scatter_dp(x, groups):
    ring, plus, minus, partner = _dp_rings(groups)
    d = lax.axis_index("dp")
    y = d // 2
    h = d % 2
    up = _take(x, 2 * ((y - 1) % ring))
    down = _take(x, 2 * ((y + 1) % ring) + 1)
    for t in range(ring - 1):
        up = lax.ppermute(up, "dp", plus)
        down = lax.ppermute(down, "dp", minus)
        up = up + _take(x, 2 * ((y - t - 2) % ring))
        down = down + _take(x, 2 * ((y + t + 2) % ring) + 1)
    keep = lax.select(h == 0, up, down)
    send = lax.select(h == 0, down, up)
    return keep + lax.ppermute(send, "dp", partner)


def _all_gather_dp(mine, groups):
    ring, plus, minus, partner = _dp_rings(groups)
    d = lax.axis_index("dp")
    y = d // 2
    h = d % 2
    other = lax.ppermute(mine, "dp", partner)
    even = lax.select(h == 0, mine, other)
    odd = lax.select(h == 0, other, mine)
    lead, block, cols = mine.shape
    out = jnp.zeros((lead, ring, 2, block, cols), mine.dtype)
    out = lax.dynamic_update_slice(out, jnp.stack([even, odd], axis=1)[:, None], (0, y, 0, 0, 0))
    up, down = even, odd
    for t in range(ring - 1):
        up = lax.ppermute(up, "dp", plus)
        down = lax.ppermute(down, "dp", minus)
        out = lax.dynamic_update_slice(out, up[:, None, None], (0, (y - t - 1) % ring, 0, 0, 0))
        out = lax.dynamic_update_slice(out, down[:, None, None], (0, (y + t + 1) % ring, 1, 0, 0))
    return out.reshape(lead, groups * block, cols)


def _adam(gradient, params, moment_one, moment_two, learn, fix_one, fix_two):
    new_one = 0.9 * moment_one + 0.1 * gradient
    new_two = 0.95 * moment_two + 0.05 * gradient * gradient
    update = new_one / fix_one / (jnp.sqrt(new_two / fix_two) + 1e-08) + 0.1 * params
    return params - learn * update, new_one, new_two


def _step(grads, params, moment_one, moment_two, relation_ids, rates, step_count):
    groups = lax.axis_size("dp")
    owners = lax.axis_size("shard")
    relations = grads.shape[1]
    rows = grads.shape[3]
    panel_cols = grads.shape[-1]
    owned = params.shape[2]
    block = rows // groups
    lead = relations * 2
    onehot = (relation_ids[:, None] == jnp.arange(rates.shape[0], dtype=jnp.int32)[None, :]).astype(
        jnp.float32
    )
    learn = jnp.sum(onehot * rates[None, :], axis=1)[:, None, None, None]
    steps = step_count[0].astype(jnp.float32)
    fix_one = 1.0 - jnp.power(jnp.float32(0.9), steps)
    fix_two = 1.0 - jnp.power(jnp.float32(0.95), steps)
    state = jnp.stack([params, moment_one, moment_two]).reshape(3, relations, 2, 1, owned, owners, panel_cols)
    state = lax.all_to_all(state, "shard", split_axis=5, concat_axis=3, tiled=True)
    state = state.reshape(3, relations, 2, block, panel_cols)
    local = grads.reshape(lead, groups, block, panel_cols)
    summed = _reduce_scatter_dp(local, groups)
    gradient = summed.reshape(relations, 2, block, panel_cols) / groups
    fresh, _, _ = _adam(gradient, state[0], state[1], state[2], learn, fix_one, fix_two)
    fresh = fresh.astype(jnp.bfloat16).reshape(lead, block, panel_cols)
    panels = _all_gather_dp(fresh, groups).reshape(relations, 2, rows, panel_cols)
    moved = (summed / groups).reshape(relations, 2, owners, owned, 1, panel_cols)
    moved = lax.all_to_all(moved, "shard", split_axis=2, concat_axis=4, tiled=True)
    moved = moved.reshape(relations, 2, owned, owners * panel_cols)
    new_params, new_one, new_two = _adam(moved, params, moment_one, moment_two, learn, fix_one, fix_two)
    return (new_params, new_one, new_two, panels)


def solution(mesh):
    in_specs = (
        P("dp", None, None, None, "shard"),
        P(None, None, ("dp", "shard"), None),
        P(None, None, ("dp", "shard"), None),
        P(None, None, ("dp", "shard"), None),
        P(),
        P(),
        P(),
    )
    out_specs = (
        P(None, None, ("dp", "shard"), None),
        P(None, None, ("dp", "shard"), None),
        P(None, None, ("dp", "shard"), None),
        P(None, None, None, "shard"),
    )
    return jax.shard_map(_step, mesh=mesh, in_specs=in_specs, out_specs=out_specs, check_vma=False)
```

```python
import jax
import jax.numpy as jnp
from jax import lax
from jax.sharding import PartitionSpec as P


def _dp_rings(groups):
    ring = groups // 2
    plus = [(2 * y + h, 2 * ((y + 1) % ring) + h) for y in range(ring) for h in range(2)]
    minus = [(2 * y + h, 2 * ((y - 1) % ring) + h) for y in range(ring) for h in range(2)]
    partner = [(2 * y + h, 2 * y + 1 - h) for y in range(ring) for h in range(2)]
    return ring, plus, minus, partner


def _take(x, index):
    return lax.dynamic_index_in_dim(x, index, axis=1, keepdims=False)


def _ring_sum(y, ring, perm, sign, pick):
    acc = pick((y - sign) % ring)
    for t in range(ring - 1):
        acc = lax.ppermute(acc, "dp", perm)
        acc = acc + pick((y - sign * (t + 2)) % ring)
    return acc


def _reduce_scatter_dp(x, groups):
    ring, plus, minus, partner = _dp_rings(groups)
    d = lax.axis_index("dp")
    y = d // 2
    h = d % 2
    half = x.shape[0] // 2
    rows = x.shape[2] // 2
    first = x[:half]
    up = _ring_sum(y, ring, plus, 1, lambda c: _take(first, 2 * c))
    down = _ring_sum(y, ring, minus, -1, lambda c: _take(first, 2 * c + 1))
    keep = lax.select(h == 0, up, down)
    send = lax.select(h == 0, down, up)
    done_first = keep + lax.ppermute(send, "dp", partner)
    second = x[half:].reshape(x.shape[0] - half, ring, 2, x.shape[2], x.shape[3])
    mine = lax.dynamic_index_in_dim(second, h, axis=2, keepdims=False)
    theirs = lax.dynamic_index_in_dim(second, 1 - h, axis=2, keepdims=False)
    paired = mine + lax.ppermute(theirs, "dp", partner)
    top = _ring_sum(y, ring, plus, 1, lambda c: _take(paired, c)[:, :rows])
    bottom = _ring_sum(y, ring, minus, -1, lambda c: _take(paired, c)[:, rows:])
    done_second = jnp.concatenate([top, bottom], axis=1)
    return jnp.concatenate([done_first, done_second], axis=0)


def _all_gather_dp(mine, groups):
    ring, plus, minus, partner = _dp_rings(groups)
    d = lax.axis_index("dp")
    y = d // 2
    h = d % 2
    other = lax.ppermute(mine, "dp", partner)
    even = lax.select(h == 0, mine, other)
    odd = lax.select(h == 0, other, mine)
    lead, block, cols = mine.shape
    out = jnp.zeros((lead, ring, 2, block, cols), mine.dtype)
    out = lax.dynamic_update_slice(out, jnp.stack([even, odd], axis=1)[:, None], (0, y, 0, 0, 0))
    up, down = even, odd
    for t in range(ring - 1):
        up = lax.ppermute(up, "dp", plus)
        down = lax.ppermute(down, "dp", minus)
        out = lax.dynamic_update_slice(out, up[:, None, None], (0, (y - t - 1) % ring, 0, 0, 0))
        out = lax.dynamic_update_slice(out, down[:, None, None], (0, (y + t + 1) % ring, 1, 0, 0))
    return out.reshape(lead, groups * block, cols)


def _adam(gradient, params, moment_one, moment_two, learn, fix_one, fix_two):
    new_one = 0.9 * moment_one + 0.1 * gradient
    new_two = 0.95 * moment_two + 0.05 * gradient * gradient
    update = new_one / fix_one / (jnp.sqrt(new_two / fix_two) + 1e-08) + 0.1 * params
    return params - learn * update, new_one, new_two


def _step(grads, params, moment_one, moment_two, relation_ids, rates, step_count):
    groups = lax.axis_size("dp")
    owners = lax.axis_size("shard")
    relations = grads.shape[1]
    rows = grads.shape[3]
    panel_cols = grads.shape[-1]
    owned = params.shape[2]
    block = rows // groups
    lead = relations * 2
    onehot = (relation_ids[:, None] == jnp.arange(rates.shape[0], dtype=jnp.int32)[None, :]).astype(
        jnp.float32
    )
    learn = jnp.sum(onehot * rates[None, :], axis=1)[:, None, None, None]
    steps = step_count[0].astype(jnp.float32)
    fix_one = 1.0 - jnp.power(jnp.float32(0.9), steps)
    fix_two = 1.0 - jnp.power(jnp.float32(0.95), steps)
    state = jnp.stack([params, moment_one, moment_two]).reshape(3, relations, 2, 1, owned, owners, panel_cols)
    state = lax.all_to_all(state, "shard", split_axis=5, concat_axis=3, tiled=True)
    state = state.reshape(3, relations, 2, block, panel_cols)
    local = grads.reshape(lead, groups, block, panel_cols)
    summed = _reduce_scatter_dp(local, groups)
    gradient = summed.reshape(relations, 2, block, panel_cols) / groups
    fresh, _, _ = _adam(gradient, state[0], state[1], state[2], learn, fix_one, fix_two)
    fresh = fresh.astype(jnp.bfloat16).reshape(lead, block, panel_cols)
    panels = _all_gather_dp(fresh, groups).reshape(relations, 2, rows, panel_cols)
    moved = (summed / groups).reshape(relations, 2, owners, owned, 1, panel_cols)
    moved = lax.all_to_all(moved, "shard", split_axis=2, concat_axis=4, tiled=True)
    moved = moved.reshape(relations, 2, owned, owners * panel_cols)
    new_params, new_one, new_two = _adam(moved, params, moment_one, moment_two, learn, fix_one, fix_two)
    return (new_params, new_one, new_two, panels)


def solution(mesh):
    in_specs = (
        P("dp", None, None, None, "shard"),
        P(None, None, ("dp", "shard"), None),
        P(None, None, ("dp", "shard"), None),
        P(None, None, ("dp", "shard"), None),
        P(),
        P(),
        P(),
    )
    out_specs = (
        P(None, None, ("dp", "shard"), None),
        P(None, None, ("dp", "shard"), None),
        P(None, None, ("dp", "shard"), None),
        P(None, None, None, "shard"),
    )
    return jax.shard_map(_step, mesh=mesh, in_specs=in_specs, out_specs=out_specs, check_vma=False)
```

```python
import jax
import jax.numpy as jnp
from jax import lax
from jax.sharding import PartitionSpec as P


def _dp_rings(groups):
    ring = groups // 2
    plus = [(2 * y + h, 2 * ((y + 1) % ring) + h) for y in range(ring) for h in range(2)]
    minus = [(2 * y + h, 2 * ((y - 1) % ring) + h) for y in range(ring) for h in range(2)]
    partner = [(2 * y + h, 2 * y + 1 - h) for y in range(ring) for h in range(2)]
    return ring, plus, minus, partner


def _take(x, index):
    return lax.dynamic_index_in_dim(x, index, axis=1, keepdims=False)


def _reduce_scatter_dp(x, groups):
    ring, plus, minus, partner = _dp_rings(groups)
    d = lax.axis_index("dp")
    y = d // 2
    h = d % 2
    up = _take(x, 2 * ((y - 1) % ring))
    down = _take(x, 2 * ((y + 1) % ring) + 1)
    for t in range(ring - 1):
        up = lax.ppermute(up, "dp", plus)
        down = lax.ppermute(down, "dp", minus)
        up = up + _take(x, 2 * ((y - t - 2) % ring))
        down = down + _take(x, 2 * ((y + t + 2) % ring) + 1)
    keep = lax.select(h == 0, up, down)
    send = lax.select(h == 0, down, up)
    return keep + lax.ppermute(send, "dp", partner)


def _all_gather_dp(mine, groups):
    ring, plus, minus, partner = _dp_rings(groups)
    d = lax.axis_index("dp")
    y = d // 2
    h = d % 2
    lead, block, cols = mine.shape
    rows = block // 2
    out = jnp.zeros((lead, ring, 2, block, cols), mine.dtype)

    def ring_along_y(piece, side):
        nonlocal out
        out = lax.dynamic_update_slice(out, piece[:, None, None], (0, y, side, 0, 0))
        top = piece[:, :rows]
        bottom = piece[:, rows:]
        for t in range(ring - 1):
            top = lax.ppermute(top, "dp", plus)
            bottom = lax.ppermute(bottom, "dp", minus)
            out = lax.dynamic_update_slice(out, top[:, None, None], (0, (y - t - 1) % ring, side, 0, 0))
            out = lax.dynamic_update_slice(out, bottom[:, None, None], (0, (y + t + 1) % ring, side, rows, 0))

    other = lax.ppermute(mine, "dp", partner)
    ring_along_y(mine, h)
    ring_along_y(other, 1 - h)
    return out.reshape(lead, groups * block, cols)


def _adam(gradient, params, moment_one, moment_two, learn, fix_one, fix_two):
    new_one = 0.9 * moment_one + 0.1 * gradient
    new_two = 0.95 * moment_two + 0.05 * gradient * gradient
    update = new_one / fix_one / (jnp.sqrt(new_two / fix_two) + 1e-08) + 0.1 * params
    return params - learn * update, new_one, new_two


def _step(grads, params, moment_one, moment_two, relation_ids, rates, step_count):
    groups = lax.axis_size("dp")
    owners = lax.axis_size("shard")
    relations = grads.shape[1]
    rows = grads.shape[3]
    panel_cols = grads.shape[-1]
    owned = params.shape[2]
    block = rows // groups
    lead = relations * 2
    onehot = (relation_ids[:, None] == jnp.arange(rates.shape[0], dtype=jnp.int32)[None, :]).astype(
        jnp.float32
    )
    learn = jnp.sum(onehot * rates[None, :], axis=1)[:, None, None, None]
    steps = step_count[0].astype(jnp.float32)
    fix_one = 1.0 - jnp.power(jnp.float32(0.9), steps)
    fix_two = 1.0 - jnp.power(jnp.float32(0.95), steps)
    state = jnp.stack([params, moment_one, moment_two]).reshape(3, relations, 2, 1, owned, owners, panel_cols)
    state = lax.all_to_all(state, "shard", split_axis=5, concat_axis=3, tiled=True)
    state = state.reshape(3, relations, 2, block, panel_cols)
    local = grads.reshape(lead, groups, block, panel_cols)
    summed = _reduce_scatter_dp(local, groups)
    gradient = summed.reshape(relations, 2, block, panel_cols) / groups
    fresh, _, _ = _adam(gradient, state[0], state[1], state[2], learn, fix_one, fix_two)
    fresh = fresh.astype(jnp.bfloat16).reshape(lead, block, panel_cols)
    panels = _all_gather_dp(fresh, groups).reshape(relations, 2, rows, panel_cols)
    moved = (summed / groups).reshape(relations, 2, owners, owned, 1, panel_cols)
    moved = lax.all_to_all(moved, "shard", split_axis=2, concat_axis=4, tiled=True)
    moved = moved.reshape(relations, 2, owned, owners * panel_cols)
    new_params, new_one, new_two = _adam(moved, params, moment_one, moment_two, learn, fix_one, fix_two)
    return (new_params, new_one, new_two, panels)


def solution(mesh):
    in_specs = (
        P("dp", None, None, None, "shard"),
        P(None, None, ("dp", "shard"), None),
        P(None, None, ("dp", "shard"), None),
        P(None, None, ("dp", "shard"), None),
        P(),
        P(),
        P(),
    )
    out_specs = (
        P(None, None, ("dp", "shard"), None),
        P(None, None, ("dp", "shard"), None),
        P(None, None, ("dp", "shard"), None),
        P(None, None, None, "shard"),
    )
    return jax.shard_map(_step, mesh=mesh, in_specs=in_specs, out_specs=out_specs, check_vma=False)
```

```python
import jax
import jax.numpy as jnp
from jax import lax
from jax.sharding import PartitionSpec as P


def _dp_rings(groups):
    ring = groups // 2
    plus = [(2 * y + h, 2 * ((y + 1) % ring) + h) for y in range(ring) for h in range(2)]
    minus = [(2 * y + h, 2 * ((y - 1) % ring) + h) for y in range(ring) for h in range(2)]
    partner = [(2 * y + h, 2 * y + 1 - h) for y in range(ring) for h in range(2)]
    return ring, plus, minus, partner


def _take(x, index):
    return lax.dynamic_index_in_dim(x, index, axis=1, keepdims=False)


def _reduce_scatter_dp(x, groups):
    ring, plus, minus, partner = _dp_rings(groups)
    d = lax.axis_index("dp")
    y = d // 2
    h = d % 2
    raw = lax.ppermute(_take(x, 2 * y + 1 - h), "dp", partner)
    up = _take(x, 2 * ((y - 1) % ring))
    down = _take(x, 2 * ((y + 1) % ring) + 1)
    for t in range(ring - 2):
        up = lax.ppermute(up, "dp", plus)
        down = lax.ppermute(down, "dp", minus)
        up = up + _take(x, 2 * ((y - t - 2) % ring))
        down = down + _take(x, 2 * ((y + t + 2) % ring) + 1)
    within = [(2 * r, 2 * ((r + 1) % ring)) for r in range(ring)]
    within += [(2 * r + 1, 2 * ((r - 1) % ring) + 1) for r in range(ring)]
    across = [(2 * r + 1, 2 * ((r + 1) % ring)) for r in range(ring)]
    across += [(2 * r, 2 * ((r - 1) % ring) + 1) for r in range(ring)]
    same = lax.ppermute(lax.select(h == 0, up, down), "dp", within)
    other = lax.ppermute(lax.select(h == 0, down, up), "dp", across)
    return (_take(x, 2 * y + h) + same) + (other + raw)


def _all_gather_dp(mine, groups):
    ring, plus, minus, partner = _dp_rings(groups)
    d = lax.axis_index("dp")
    y = d // 2
    h = d % 2
    lead, block, cols = mine.shape
    within = [(2 * r, 2 * ((r + 1) % ring)) for r in range(ring)]
    within += [(2 * r + 1, 2 * ((r - 1) % ring) + 1) for r in range(ring)]
    across = [(2 * r, 2 * ((r + 1) % ring) + 1) for r in range(ring)]
    across += [(2 * r + 1, 2 * ((r - 1) % ring)) for r in range(ring)]
    other = lax.ppermute(mine, "dp", partner)
    same = lax.ppermute(mine, "dp", within)
    diagonal = lax.ppermute(mine, "dp", across)
    up = lax.select(h == 0, same, diagonal)
    down = lax.select(h == 0, diagonal, same)
    out = jnp.zeros((lead, ring, 2, block, cols), mine.dtype)
    out = lax.dynamic_update_slice(out, mine[:, None, None], (0, y, h, 0, 0))
    out = lax.dynamic_update_slice(out, other[:, None, None], (0, y, 1 - h, 0, 0))
    for t in range(ring - 1):
        if t:
            up = lax.ppermute(up, "dp", plus)
            down = lax.ppermute(down, "dp", minus)
        out = lax.dynamic_update_slice(out, up[:, None, None], (0, (y - t - 1) % ring, 0, 0, 0))
        out = lax.dynamic_update_slice(out, down[:, None, None], (0, (y + t + 1) % ring, 1, 0, 0))
    return out.reshape(lead, groups * block, cols)


def _adam(gradient, params, moment_one, moment_two, learn, fix_one, fix_two):
    new_one = 0.9 * moment_one + 0.1 * gradient
    new_two = 0.95 * moment_two + 0.05 * gradient * gradient
    update = new_one / fix_one / (jnp.sqrt(new_two / fix_two) + 1e-08) + 0.1 * params
    return params - learn * update, new_one, new_two


def _step(grads, params, moment_one, moment_two, relation_ids, rates, step_count):
    groups = lax.axis_size("dp")
    owners = lax.axis_size("shard")
    relations = grads.shape[1]
    rows = grads.shape[3]
    panel_cols = grads.shape[-1]
    owned = params.shape[2]
    block = rows // groups
    lead = relations * 2
    onehot = (relation_ids[:, None] == jnp.arange(rates.shape[0], dtype=jnp.int32)[None, :]).astype(
        jnp.float32
    )
    learn = jnp.sum(onehot * rates[None, :], axis=1)[:, None, None, None]
    steps = step_count[0].astype(jnp.float32)
    fix_one = 1.0 - jnp.power(jnp.float32(0.9), steps)
    fix_two = 1.0 - jnp.power(jnp.float32(0.95), steps)
    state = jnp.stack([params, moment_one, moment_two]).reshape(3, relations, 2, 1, owned, owners, panel_cols)
    state = lax.all_to_all(state, "shard", split_axis=5, concat_axis=3, tiled=True)
    state = state.reshape(3, relations, 2, block, panel_cols)
    local = grads.reshape(lead, groups, block, panel_cols)
    summed = _reduce_scatter_dp(local, groups)
    gradient = summed.reshape(relations, 2, block, panel_cols) / groups
    fresh, _, _ = _adam(gradient, state[0], state[1], state[2], learn, fix_one, fix_two)
    fresh = fresh.astype(jnp.bfloat16).reshape(lead, block, panel_cols)
    panels = _all_gather_dp(fresh, groups).reshape(relations, 2, rows, panel_cols)
    moved = (summed / groups).reshape(relations, 2, owners, owned, 1, panel_cols)
    moved = lax.all_to_all(moved, "shard", split_axis=2, concat_axis=4, tiled=True)
    moved = moved.reshape(relations, 2, owned, owners * panel_cols)
    new_params, new_one, new_two = _adam(moved, params, moment_one, moment_two, learn, fix_one, fix_two)
    return (new_params, new_one, new_two, panels)


def solution(mesh):
    in_specs = (
        P("dp", None, None, None, "shard"),
        P(None, None, ("dp", "shard"), None),
        P(None, None, ("dp", "shard"), None),
        P(None, None, ("dp", "shard"), None),
        P(),
        P(),
        P(),
    )
    out_specs = (
        P(None, None, ("dp", "shard"), None),
        P(None, None, ("dp", "shard"), None),
        P(None, None, ("dp", "shard"), None),
        P(None, None, None, "shard"),
    )
    return jax.shard_map(_step, mesh=mesh, in_specs=in_specs, out_specs=out_specs, check_vma=False)
```

```python
import jax
import jax.numpy as jnp
from jax import lax
from jax.sharding import PartitionSpec as P


def _dp_rings(groups):
    ring = groups // 2
    plus = [(2 * y + h, 2 * ((y + 1) % ring) + h) for y in range(ring) for h in range(2)]
    minus = [(2 * y + h, 2 * ((y - 1) % ring) + h) for y in range(ring) for h in range(2)]
    partner = [(2 * y + h, 2 * y + 1 - h) for y in range(ring) for h in range(2)]
    return ring, plus, minus, partner


def _take(x, index):
    return lax.dynamic_index_in_dim(x, index, axis=1, keepdims=False)


def _reduce_scatter_dp(x, groups):
    ring, plus, minus, partner = _dp_rings(groups)
    d = lax.axis_index("dp")
    y = d // 2
    h = d % 2
    raw = lax.ppermute(_take(x, 2 * y + 1 - h), "dp", partner)
    up = _take(x, 2 * ((y - 1) % ring))
    down = _take(x, 2 * ((y + 1) % ring) + 1)
    for t in range(ring - 2):
        up = lax.ppermute(up, "dp", plus)
        down = lax.ppermute(down, "dp", minus)
        up = up + _take(x, 2 * ((y - t - 2) % ring))
        down = down + _take(x, 2 * ((y + t + 2) % ring) + 1)
    within = [(2 * r, 2 * ((r + 1) % ring)) for r in range(ring)]
    within += [(2 * r + 1, 2 * ((r - 1) % ring) + 1) for r in range(ring)]
    across = [(2 * r + 1, 2 * ((r + 1) % ring)) for r in range(ring)]
    across += [(2 * r, 2 * ((r - 1) % ring) + 1) for r in range(ring)]
    same = lax.ppermute(lax.select(h == 0, up, down), "dp", within)
    other = lax.ppermute(lax.select(h == 0, down, up), "dp", across)
    return (_take(x, 2 * y + h) + same) + (other + raw)


def _all_gather_dp(mine, groups):
    ring, plus, minus, partner = _dp_rings(groups)
    d = lax.axis_index("dp")
    y = d // 2
    h = d % 2
    other = lax.ppermute(mine, "dp", partner)
    even = lax.select(h == 0, mine, other)
    odd = lax.select(h == 0, other, mine)
    lead, block, cols = mine.shape
    out = jnp.zeros((lead, ring, 2, block, cols), mine.dtype)
    out = lax.dynamic_update_slice(out, jnp.stack([even, odd], axis=1)[:, None], (0, y, 0, 0, 0))
    up, down = even, odd
    for t in range(ring - 1):
        up = lax.ppermute(up, "dp", plus)
        down = lax.ppermute(down, "dp", minus)
        out = lax.dynamic_update_slice(out, up[:, None, None], (0, (y - t - 1) % ring, 0, 0, 0))
        out = lax.dynamic_update_slice(out, down[:, None, None], (0, (y + t + 1) % ring, 1, 0, 0))
    return out.reshape(lead, groups * block, cols)


def _adam(gradient, params, moment_one, moment_two, learn, fix_one, fix_two):
    new_one = 0.9 * moment_one + 0.1 * gradient
    new_two = 0.95 * moment_two + 0.05 * gradient * gradient
    update = new_one / fix_one / (jnp.sqrt(new_two / fix_two) + 1e-08) + 0.1 * params
    return params - learn * update, new_one, new_two


def _step(grads, params, moment_one, moment_two, relation_ids, rates, step_count):
    groups = lax.axis_size("dp")
    owners = lax.axis_size("shard")
    relations = grads.shape[1]
    rows = grads.shape[3]
    panel_cols = grads.shape[-1]
    owned = params.shape[2]
    block = rows // groups
    lead = relations * 2
    onehot = (relation_ids[:, None] == jnp.arange(rates.shape[0], dtype=jnp.int32)[None, :]).astype(
        jnp.float32
    )
    learn = jnp.sum(onehot * rates[None, :], axis=1)[:, None, None, None]
    steps = step_count[0].astype(jnp.float32)
    fix_one = 1.0 - jnp.power(jnp.float32(0.9), steps)
    fix_two = 1.0 - jnp.power(jnp.float32(0.95), steps)
    state = jnp.stack([params, moment_one, moment_two]).reshape(3, relations, 2, 1, owned, owners, panel_cols)
    state = lax.all_to_all(state, "shard", split_axis=5, concat_axis=3, tiled=True)
    state = state.reshape(3, relations, 2, block, panel_cols)
    local = grads.reshape(lead, groups, block, panel_cols)
    summed = _reduce_scatter_dp(local, groups)
    gradient = summed.reshape(relations, 2, block, panel_cols) / groups
    fresh, _, _ = _adam(gradient, state[0], state[1], state[2], learn, fix_one, fix_two)
    fresh = fresh.astype(jnp.bfloat16).reshape(lead, block, panel_cols)
    panels = _all_gather_dp(fresh, groups).reshape(relations, 2, rows, panel_cols)
    moved = (summed / groups).reshape(relations, 2, owners, owned, 1, panel_cols)
    moved = lax.all_to_all(moved, "shard", split_axis=2, concat_axis=4, tiled=True)
    moved = moved.reshape(relations, 2, owned, owners * panel_cols)
    new_params, new_one, new_two = _adam(moved, params, moment_one, moment_two, learn, fix_one, fix_two)
    return (new_params, new_one, new_two, panels)


def solution(mesh):
    in_specs = (
        P("dp", None, None, None, "shard"),
        P(None, None, ("dp", "shard"), None),
        P(None, None, ("dp", "shard"), None),
        P(None, None, ("dp", "shard"), None),
        P(),
        P(),
        P(),
    )
    out_specs = (
        P(None, None, ("dp", "shard"), None),
        P(None, None, ("dp", "shard"), None),
        P(None, None, ("dp", "shard"), None),
        P(None, None, None, "shard"),
    )
    return jax.shard_map(_step, mesh=mesh, in_specs=in_specs, out_specs=out_specs, check_vma=False)
```
